128 devices in a mesh: ctx: 8 (over y, core), head: 16 (over z, x).
Axes of the slice: x: 4, y: 4, z: 4, core: 2. Of those that a mesh axis runs over, the one named last changes fastest.
Arguments:
- conv_input: bfloat16 [32768, 20480], P(('ctx', 'head')), may hold values from -6 to 6
- dt_raw: bfloat16 [32768, 256], P(('ctx', 'head')), as said below
- conv_weight: bfloat16 [4, 20480], replicated, may hold values from -3 to 3
- conv_bias: float32 [20480], replicated, may hold values from -3 to 3
- a_log: float32 [256], replicated, may hold values from -0.2 to 0.2
- dt_bias: float32 [256], replicated, as said below
- d_skip: float32 [256], replicated, may hold values from 0.5 to 1.5
Outputs:
- scan_out: bfloat16 [32768, 16384], P('ctx', 'head')
The draws below stay inside these ranges and needn't reach their ends.
Inputs may be any that keep to these rules, and one draw needn't show every extreme that they name: softplus(dt_bias[h]) lies between 0.02 / 32768 and 0.04 for every head. softplus(dt_raw[t, h] + dt_bias[h]) lies between 0.02 / 32768 and 0.5 for every token and head.
All inputs are finite; a program needn't handle non-finite values.
Results may differ from the reference program's by a relative error of at most 0.0046.
Values may be sent and summed in bfloat16 or wider, within the bound.
No kernel may reach another device: no remote copies, remote signals or barrier semaphores. Data moves between devices by JAX's collectives and lax.ppermute only.
A program may use at most 256 MiB of HBM per device.

```python
import jax
import jax.numpy as jnp
from jax import lax

HEADS = 256
HEADDIM = 64
STATE = 256
GROUPS = 8
CONV = 4
SPAN = 512
TOK_DEV = 256
INPUT_LENGTH = 32768
XBCW = 20480


def head_profile(key):
    first, second, third = jax.random.split(jax.random.fold_in(key, 7), 3)
    share = 0.5
    gradual_trend = jax.random.uniform(first, (HEADS,), jnp.float32) < share
    fast_step = jax.random.uniform(second, (HEADS,), jnp.float32, 0.02, 0.035)
    slow_step = jax.random.uniform(third, (HEADS,), jnp.float32, 0.1, 0.3) / INPUT_LENGTH
    constant_floor = jnp.where(gradual_trend, jnp.log(slow_step), jnp.log(fast_step))
    return (gradual_trend, constant_floor)


def draw_dt_bias(key, part):
    gradual_trend, constant_floor = head_profile(key)
    return constant_floor.astype(jnp.float32)


def draw_dt_raw(key, part):
    gradual_trend, constant_floor = head_profile(key)
    first, second, third = jax.random.split(jax.random.fold_in(key, 11), 3)
    noise_term = jnp.clip(0.5 * jax.random.normal(first, (INPUT_LENGTH, HEADS), jnp.float32), -1.2, 1.2)
    displacement_amounts = jax.random.uniform(second, (INPUT_LENGTH // TOK_DEV, HEADS), jnp.float32, -0.35, 0.35)
    displacement_amounts = jnp.repeat(displacement_amounts, TOK_DEV, axis=0)
    impulse_indices = jnp.arange(8, dtype=jnp.int32) * (INPUT_LENGTH // 8) + jax.random.randint(third, (8,), 0, INPUT_LENGTH // 8)
    impulse_height = jnp.any(jnp.arange(INPUT_LENGTH, dtype=jnp.int32)[:, None] == impulse_indices[None, :], axis=1)
    sequence_samples = jnp.where(impulse_height[:, None] & gradual_trend[None, :], -1.5 - constant_floor[None, :], noise_term + displacement_amounts)
    return sequence_samples.astype(jnp.bfloat16)


def shard_levels(key, dims, cuts, smallest, top_value):
    gain, own = 1.0, jax.random.fold_in(key, 6)
    for axis_at, shards_of in cuts:
        heights = jnp.exp(jax.random.uniform(jax.random.fold_in(own, axis_at), (shards_of,), jnp.float32, smallest / len(cuts), top_value / len(cuts)))
        gain = gain * jnp.repeat(heights, dims[axis_at] // shards_of).reshape([-1 if axis == axis_at else 1 for axis in range(len(dims))])
    return gain


def scatter_about(rng, shape, spread, reach, shards=(), held_as=jnp.bfloat16):
    array = spread * jax.random.normal(rng, shape, jnp.float32)
    if shards:
        array = array * shard_levels(rng, shape, shards, -0.22, 0.18)
    return jnp.clip(array, -reach, reach).astype(held_as)


def setup_inputs(seed: int = 0) -> dict:
    splits = jax.random.split(jax.random.key(seed), 8)
    conv_input = scatter_about(splits[0], (INPUT_LENGTH, XBCW), 1.0, 6.0, ((0, 128),))
    dt_raw = draw_dt_raw(jax.random.fold_in(splits[7], 71), 0)
    conv_weight = scatter_about(splits[2], (CONV, XBCW), CONV ** -0.5, 3.0)
    conv_bias = scatter_about(splits[3], (XBCW,), 0.5, 3.0, (), jnp.float32)
    a_log = jnp.clip(jax.random.uniform(splits[4], (HEADS,), jnp.float32, -0.2, 0.2), -0.2, 0.2)
    dt_bias = draw_dt_bias(jax.random.fold_in(splits[7], 71), 0)
    d_skip = jnp.clip(1.0 + 0.1 * jax.random.normal(splits[6], (HEADS,), jnp.float32), 0.5, 1.5)
    return {"conv_input": conv_input, "dt_raw": dt_raw, "conv_weight": conv_weight, "conv_bias": conv_bias, "a_log": a_log, "dt_bias": dt_bias, "d_skip": d_skip}


def reference(conv_input, dt_raw, conv_weight, conv_bias, a_log, dt_bias, d_skip):
    f32 = jnp.float32
    x_width = HEADS * HEADDIM
    per_group = HEADS // GROUPS
    width = conv_input.shape[1]
    padded = jnp.concatenate([jnp.zeros((CONV - 1, width), conv_input.dtype), conv_input], 0)
    taps = conv_weight.astype(f32)
    rate = -jnp.exp(a_log)
    tri = lax.broadcasted_iota(jnp.int32, (SPAN, SPAN), 0) >= lax.broadcasted_iota(jnp.int32, (SPAN, SPAN), 1)
    blocks = INPUT_LENGTH // SPAN

    def one_block(state, index):
        start = (index * SPAN).astype(jnp.int32)
        window = lax.dynamic_slice_in_dim(padded, start, SPAN + CONV - 1, 0).astype(f32)
        total = window[0:SPAN] * taps[0]
        for k in range(1, CONV):
            total = total + window[k:k + SPAN] * taps[k]
        act = jax.nn.silu(total + conv_bias).astype(jnp.bfloat16)
        x_act = act[:, :x_width]
        b_act = act[:, x_width:x_width + GROUPS * STATE].reshape(SPAN, GROUPS, STATE).astype(f32)
        c_act = act[:, x_width + GROUPS * STATE:].reshape(SPAN, GROUPS, STATE).astype(f32)
        raw = lax.dynamic_slice_in_dim(dt_raw, start, SPAN, 0).astype(f32)
        step = jax.nn.softplus(raw + dt_bias)
        cum = jnp.cumsum(rate * step, axis=0)
        grams = jnp.einsum('tgn,sgn->gts', c_act, b_act)
        grams = jnp.repeat(grams, per_group, axis=0)
        cum_t = cum.T
        decay = jnp.exp(jnp.where(tri[None], cum_t[:, :, None] - cum_t[:, None, :], -jnp.inf))
        mix = (grams * decay * step.T[:, None, :]).astype(jnp.bfloat16)
        x_heads = x_act.reshape(SPAN, HEADS, HEADDIM).astype(f32)
        y_block = jnp.einsum('hts,shp->thp', mix.astype(f32), x_heads).reshape(SPAN, x_width)
        grown = jnp.repeat(jnp.exp(cum), HEADDIM, axis=1)
        y_state = grown * jnp.einsum('tgn,ngc->tgc', c_act, state.reshape(STATE, GROUPS, per_group * HEADDIM), precision=lax.Precision.HIGHEST).reshape(SPAN, x_width)
        weight = jnp.exp(cum[-1][None, :] - cum) * step
        xw = (x_heads * weight[:, :, None]).astype(jnp.bfloat16).astype(f32)
        contrib = jnp.einsum('sgn,sgc->ngc', b_act, xw.reshape(SPAN, GROUPS, per_group * HEADDIM)).reshape(STATE, x_width)
        fade = jnp.exp(jnp.repeat(cum[-1], HEADDIM))
        new_state = state * fade[None, :] + contrib
        skip = jnp.repeat(d_skip, HEADDIM)
        out = (y_block + y_state + skip * x_act.astype(f32)).astype(jnp.bfloat16)
        return new_state, out

    start_state = jnp.zeros((STATE, x_width), f32)
    final, outs = lax.scan(one_block, start_state, jnp.arange(blocks, dtype=jnp.int32))
    return outs.reshape(INPUT_LENGTH, x_width)
```

```python
import jax
import jax.numpy as jnp
from jax import lax
from jax.sharding import PartitionSpec as P

HEADS = 256
HEADDIM = 64
STATE = 256
GROUPS = 8
CONV = 4
SPAN = 512


def shifted(value, axis, by):
    size = lax.axis_size(axis)
    pairs = [(i, i + by) for i in range(size) if 0 <= i + by < size]
    return lax.ppermute(value, axis, pairs)


def on_device(conv_input, dt_raw, conv_weight, conv_bias, a_log, dt_bias, d_skip):
    f32 = jnp.float32
    head_count = lax.axis_size("head")
    heads_dev = HEADS // head_count
    repeat_count = head_count // GROUPS
    head_pos = lax.axis_index("head")
    group = head_pos // repeat_count
    rows = conv_input.shape[0]
    x_width = HEADS * HEADDIM
    slab = heads_dev * HEADDIM
    x_part = conv_input[:, :x_width].reshape(rows, head_count, slab)
    bc = conv_input[:, x_width:].reshape(rows, 2, GROUPS, STATE)
    b_part = jnp.repeat(bc[:, 0], repeat_count, axis=1)
    c_part = jnp.repeat(bc[:, 1], repeat_count, axis=1)
    send = jnp.concatenate([x_part, b_part, c_part], axis=2)
    step_part = dt_raw.reshape(rows, head_count, heads_dev)
    arrived, steps = (
        lax.all_to_all(send, "head", split_axis=1, concat_axis=0, tiled=True),
        lax.all_to_all(step_part, "head", split_axis=1, concat_axis=0, tiled=True),
    )
    length = arrived.shape[0]
    width = slab + 2 * STATE
    local = arrived.reshape(length, width)
    steps = steps.reshape(length, heads_dev)

    def columns(table):
        last = table.ndim - 1
        return jnp.concatenate(
            [
                lax.dynamic_slice_in_dim(table, head_pos * slab, slab, last),
                lax.dynamic_slice_in_dim(table, x_width + group * STATE, STATE, last),
                lax.dynamic_slice_in_dim(table, x_width + (GROUPS + group) * STATE, STATE, last),
            ],
            last,
        )

    kernel = columns(conv_weight).astype(f32)
    offset = columns(conv_bias)
    rim = shifted(local[length - (CONV - 1) :], "ctx", 1)
    padded = jnp.concatenate([rim, local], 0)
    total = padded[0:length].astype(f32) * kernel[0]
    for k in range(1, CONV):
        total = total + padded[k : k + length].astype(f32) * kernel[k]
    act = jax.nn.silu(total + offset).astype(jnp.bfloat16)
    rate = -jnp.exp(lax.dynamic_slice_in_dim(a_log, head_pos * heads_dev, heads_dev, 0))
    bias = lax.dynamic_slice_in_dim(dt_bias, head_pos * heads_dev, heads_dev, 0)
    skip = jnp.repeat(lax.dynamic_slice_in_dim(d_skip, head_pos * heads_dev, heads_dev, 0), HEADDIM)
    step = jax.nn.softplus(steps.astype(f32) + bias)
    blocks = length // SPAN
    x_blocks = act[:, :slab].reshape(blocks, SPAN, slab)
    b_blocks = act[:, slab : slab + STATE].reshape(blocks, SPAN, STATE)
    c_blocks = act[:, slab + STATE :].reshape(blocks, SPAN, STATE)
    step_blocks = step.reshape(blocks, SPAN, heads_dev)
    cum = jnp.cumsum((rate * step).reshape(blocks, SPAN, heads_dev), axis=1)
    tri = lax.broadcasted_iota(jnp.int32, (SPAN, SPAN), 0) >= lax.broadcasted_iota(
        jnp.int32, (SPAN, SPAN), 1
    )

    def local_block(state, inputs):
        x_now, b_now, c_now, step_now, cum_now = inputs
        gram = jnp.dot(c_now, b_now.T, preferred_element_type=f32)
        cum_t = cum_now.T
        decay = jnp.exp(jnp.where(tri[None], cum_t[:, :, None] - cum_t[:, None, :], -jnp.inf))
        mix = (gram[None] * decay * step_now.T[:, None, :]).astype(jnp.bfloat16)
        x_heads = x_now.reshape(SPAN, heads_dev, HEADDIM)
        y_block = jnp.einsum("hts,shp->thp", mix, x_heads, preferred_element_type=f32).reshape(
            SPAN, slab
        )
        grown = jnp.repeat(jnp.exp(cum_now), HEADDIM, axis=1)
        y_state = grown * jnp.dot(
            c_now.astype(f32), state, precision=lax.Precision.HIGHEST, preferred_element_type=f32
        )
        y_now = y_block + y_state + skip * x_now.astype(f32)
        weight = jnp.exp(cum_now[-1][None, :] - cum_now) * step_now
        xw = (x_heads.astype(f32) * weight[:, :, None]).astype(jnp.bfloat16).reshape(SPAN, slab)
        contrib = jnp.einsum("sn,sc->nc", b_now, xw, preferred_element_type=f32)
        fade = jnp.exp(jnp.repeat(cum_now[-1], HEADDIM))
        return (state * fade[None, :] + contrib, y_now)

    start_state = jnp.zeros((STATE, slab), f32)
    final, y_blocks = lax.scan(
        local_block, start_state, (x_blocks, b_blocks, c_blocks, step_blocks, cum)
    )
    block_totals = cum[:, -1, :]
    totals = jnp.sum(block_totals, axis=0)
    tail = jnp.broadcast_to(jnp.repeat(totals, HEADDIM)[None, :], (8, slab))
    gathered = lax.all_gather(jnp.concatenate([final, tail], 0), "ctx")
    shards = gathered.shape[0]
    position = lax.axis_index("ctx")
    finals = gathered[:, :STATE]
    shard_totals = gathered[:, STATE]
    before_shard = jnp.cumsum(shard_totals, axis=0) - shard_totals
    reach = jnp.sum(jnp.where(jnp.arange(shards)[:, None] < position, shard_totals, 0.0), axis=0)
    after_own = before_shard + shard_totals
    live = jnp.arange(shards)[:, None] < position
    weights = jnp.where(live, jnp.exp(jnp.where(live, reach[None] - after_own, 0.0)), 0.0)
    incoming = jnp.sum(weights[:, None, :] * finals, axis=0)
    before = jnp.concatenate(
        [jnp.zeros((1, heads_dev), f32), jnp.cumsum(block_totals, axis=0)[:-1]], 0
    )
    lifted = jnp.exp(jnp.repeat(cum + before[:, None, :], HEADDIM, axis=2))
    y_in = lifted * jnp.einsum(
        "bqn,nc->bqc", c_blocks.astype(f32), incoming, precision=lax.Precision.HIGHEST
    )
    result = y_blocks + y_in
    return result.astype(jnp.bfloat16).reshape(length, slab)


def solution(mesh):
    placed = (P(("ctx", "head"), None), P(("ctx", "head"), None), P(), P(), P(), P(), P())
    return jax.shard_map(
        on_device, mesh=mesh, in_specs=placed, out_specs=P("ctx", "head"), check_vma=False
    )
```

```python
import jax
import jax.numpy as jnp
from jax import lax
from jax.sharding import PartitionSpec as P

HEADS = 256
HEADDIM = 64
STATE = 256
GROUPS = 8
CONV = 4
SPAN = 512


def on_device(conv_input, dt_raw, conv_weight, conv_bias, a_log, dt_bias, d_skip):
    f32 = jnp.float32
    head_count = lax.axis_size("head")
    ctx_count = lax.axis_size("ctx")
    heads_dev = HEADS // head_count
    repeat_count = head_count // GROUPS
    head_pos = lax.axis_index("head")
    rows = conv_input.shape[0]
    x_width = HEADS * HEADDIM
    slab = heads_dev * HEADDIM
    devices = ctx_count * head_count
    rim = lax.ppermute(
        conv_input[rows - (CONV - 1) :], ("ctx", "head"), [(i, i + 1) for i in range(devices - 1)]
    )
    padded = jnp.concatenate([rim, conv_input], 0)
    taps = conv_weight.astype(f32)
    total = padded[0:rows].astype(f32) * taps[0]
    for k in range(1, CONV):
        total = total + padded[k : k + rows].astype(f32) * taps[k]
    act = jax.nn.silu(total + conv_bias).astype(jnp.bfloat16)

    def payload(target):
        group = target // repeat_count
        return jnp.concatenate(
            [
                lax.dynamic_slice_in_dim(act, target * slab, slab, 1),
                lax.dynamic_slice_in_dim(act, x_width + group * STATE, STATE, 1),
                lax.dynamic_slice_in_dim(act, x_width + (GROUPS + group) * STATE, STATE, 1),
                lax.dynamic_slice_in_dim(dt_raw, target * heads_dev, heads_dev, 1),
            ],
            1,
        )

    rate = -jnp.exp(lax.dynamic_slice_in_dim(a_log, head_pos * heads_dev, heads_dev, 0))
    bias = lax.dynamic_slice_in_dim(dt_bias, head_pos * heads_dev, heads_dev, 0)
    skip = jnp.repeat(lax.dynamic_slice_in_dim(d_skip, head_pos * heads_dev, heads_dev, 0), HEADDIM)
    tri = lax.broadcasted_iota(jnp.int32, (SPAN, SPAN), 0) >= lax.broadcasted_iota(
        jnp.int32, (SPAN, SPAN), 1
    )
    pairs = head_count // 2
    blocks = pairs
    parity = head_pos % 2
    y_acc = jnp.zeros((blocks, SPAN, slab), f32)
    c_acc = jnp.zeros((blocks, SPAN, STATE), jnp.bfloat16)
    cum_acc = jnp.zeros((blocks, SPAN, heads_dev), f32)
    contrib_acc = jnp.zeros((blocks, STATE, slab), f32)
    done = []
    for m in range(blocks):
        same = [(i, 2 * ((i // 2 + m) % pairs) + i % 2) for i in range(head_count)]
        other = [(i, 2 * ((i // 2 + m) % pairs) + 1 - i % 2) for i in range(head_count)]
        t_same = 2 * ((head_pos // 2 + m) % pairs) + parity
        t_other = 2 * ((head_pos // 2 + m) % pairs) + 1 - parity
        p_same, p_other = payload(t_same), payload(t_other)
        if m >= 2:
            p_same, p_other, _ = lax.optimization_barrier((p_same, p_other, done[m - 2]))
        r_same = lax.ppermute(p_same, "head", same)
        r_other = lax.ppermute(p_other, "head", other)
        first = jnp.where(parity == 0, r_same, r_other)
        second = jnp.where(parity == 0, r_other, r_same)
        blk = jnp.concatenate([first, second], 0)
        k = (head_pos // 2 - m) % pairs
        x_now = blk[:, :slab]
        b_now = blk[:, slab : slab + STATE]
        c_now = blk[:, slab + STATE : slab + 2 * STATE]
        step_now = jax.nn.softplus(blk[:, slab + 2 * STATE :].astype(f32) + bias)
        cum_now = jnp.cumsum(rate * step_now, axis=0)
        gram = jnp.dot(c_now, b_now.T, preferred_element_type=f32)
        cum_t = cum_now.T
        decay = jnp.exp(jnp.where(tri[None], cum_t[:, :, None] - cum_t[:, None, :], -jnp.inf))
        mix = (gram[None] * decay * step_now.T[:, None, :]).astype(jnp.bfloat16)
        x_heads = x_now.reshape(SPAN, heads_dev, HEADDIM)
        y_block = jnp.einsum("hts,shp->thp", mix, x_heads, preferred_element_type=f32).reshape(
            SPAN, slab
        )
        y_now = y_block + skip * x_now.astype(f32)
        weight = jnp.exp(cum_now[-1][None, :] - cum_now) * step_now
        xw = (x_heads.astype(f32) * weight[:, :, None]).astype(jnp.bfloat16).reshape(SPAN, slab)
        contrib = jnp.einsum("sn,sc->nc", b_now, xw, preferred_element_type=f32)
        y_acc = lax.dynamic_update_index_in_dim(y_acc, y_now, k, 0)
        c_acc = lax.dynamic_update_index_in_dim(c_acc, c_now, k, 0)
        cum_acc = lax.dynamic_update_index_in_dim(cum_acc, cum_now, k, 0)
        contrib_acc = lax.dynamic_update_index_in_dim(contrib_acc, contrib, k, 0)
        done.append((contrib, y_now))

    block_totals = cum_acc[:, -1, :]
    state = jnp.zeros((STATE, slab), f32)
    entering = []
    for k in range(blocks):
        entering.append(state)
        fade = jnp.exp(jnp.repeat(block_totals[k], HEADDIM))
        state = state * fade[None, :] + contrib_acc[k]
    final = state
    entering = jnp.stack(entering)
    totals = jnp.sum(block_totals, axis=0)
    tail = jnp.broadcast_to(jnp.repeat(totals, HEADDIM)[None, :], (8, slab))
    gathered = lax.all_gather(jnp.concatenate([final, tail], 0), "ctx")
    shards = gathered.shape[0]
    position = lax.axis_index("ctx")
    finals = gathered[:, :STATE]
    shard_totals = gathered[:, STATE]
    before_shard = jnp.cumsum(shard_totals, axis=0) - shard_totals
    reach = jnp.sum(jnp.where(jnp.arange(shards)[:, None] < position, shard_totals, 0.0), axis=0)
    after_own = before_shard + shard_totals
    live = jnp.arange(shards)[:, None] < position
    weights = jnp.where(live, jnp.exp(jnp.where(live, reach[None] - after_own, 0.0)), 0.0)
    incoming = jnp.sum(weights[:, None, :] * finals, axis=0)
    before = jnp.concatenate(
        [jnp.zeros((1, heads_dev), f32), jnp.cumsum(block_totals, axis=0)[:-1]], 0
    )
    carried = jnp.exp(jnp.repeat(before, HEADDIM, axis=1))[:, None, :] * incoming[None]
    full_state = entering + carried
    grown = jnp.exp(jnp.repeat(cum_acc, HEADDIM, axis=2))
    y_state = grown * jnp.einsum(
        "bqn,bnc->bqc", c_acc.astype(f32), full_state, precision=lax.Precision.HIGHEST
    )
    result = y_acc + y_state
    return result.astype(jnp.bfloat16).reshape(blocks * SPAN, slab)


def solution(mesh):
    placed = (P(("ctx", "head"), None), P(("ctx", "head"), None), P(), P(), P(), P(), P())
    return jax.shard_map(
        on_device, mesh=mesh, in_specs=placed, out_specs=P("ctx", "head"), check_vma=False
    )
```

```python
import jax
import jax.numpy as jnp
from jax import lax
from jax.sharding import PartitionSpec as P

HEADS = 256
HEADDIM = 64
STATE = 256
GROUPS = 8
CONV = 4
SPAN = 512
CHUNKS = 4


def shifted(value, axis, by):
    size = lax.axis_size(axis)
    pairs = [(i, i + by) for i in range(size) if 0 <= i + by < size]
    return lax.ppermute(value, axis, pairs)


def convolve(local, kernel, offset):
    length = local.shape[0]
    rim = shifted(local[length - (CONV - 1) :], "ctx", 1)
    padded = jnp.concatenate([rim, local], 0)
    total = padded[0:length].astype(jnp.float32) * kernel[0]
    for k in range(1, CONV):
        total = total + padded[k : k + length].astype(jnp.float32) * kernel[k]
    return jax.nn.silu(total + offset).astype(jnp.bfloat16)


def on_device(conv_input, dt_raw, conv_weight, conv_bias, a_log, dt_bias, d_skip):
    f32 = jnp.float32
    head_count = lax.axis_size("head")
    heads_dev = HEADS // head_count
    repeat_count = head_count // GROUPS
    head_pos = lax.axis_index("head")
    group = head_pos // repeat_count
    rows = conv_input.shape[0]
    x_width = HEADS * HEADDIM
    slab = heads_dev * HEADDIM
    part_heads = heads_dev // CHUNKS
    part = part_heads * HEADDIM
    x_part = conv_input[:, :x_width].reshape(rows, head_count, slab)
    bc = conv_input[:, x_width:].reshape(rows, 2, GROUPS, STATE)
    b_part = jnp.repeat(bc[:, 0], repeat_count, axis=1)
    c_part = jnp.repeat(bc[:, 1], repeat_count, axis=1)
    step_part = dt_raw.reshape(rows, head_count, heads_dev)
    steps = lax.all_to_all(step_part, "head", split_axis=1, concat_axis=0, tiled=True)
    length = steps.shape[0]
    steps = steps.reshape(length, heads_dev)
    sends = [jnp.concatenate([b_part, c_part, x_part[:, :, :part]], axis=2)]
    for c in range(1, CHUNKS):
        sends.append(x_part[:, :, c * part : (c + 1) * part])
    arrived = []
    for s in sends:
        if arrived:
            s, _ = lax.optimization_barrier((s, arrived[-1]))
        got = lax.all_to_all(s, "head", split_axis=1, concat_axis=0, tiled=True)
        arrived.append(got.reshape(length, -1))

    taps = conv_weight.astype(f32)
    x_taps = lax.dynamic_slice_in_dim(taps, head_pos * slab, slab, 1)
    x_bias = lax.dynamic_slice_in_dim(conv_bias, head_pos * slab, slab, 0)
    bc_taps = jnp.concatenate(
        [
            lax.dynamic_slice_in_dim(taps, x_width + group * STATE, STATE, 1),
            lax.dynamic_slice_in_dim(taps, x_width + (GROUPS + group) * STATE, STATE, 1),
        ],
        1,
    )
    bc_bias = jnp.concatenate(
        [
            lax.dynamic_slice_in_dim(conv_bias, x_width + group * STATE, STATE, 0),
            lax.dynamic_slice_in_dim(conv_bias, x_width + (GROUPS + group) * STATE, STATE, 0),
        ],
        0,
    )
    rate = -jnp.exp(lax.dynamic_slice_in_dim(a_log, head_pos * heads_dev, heads_dev, 0))
    bias = lax.dynamic_slice_in_dim(dt_bias, head_pos * heads_dev, heads_dev, 0)
    skip = jnp.repeat(lax.dynamic_slice_in_dim(d_skip, head_pos * heads_dev, heads_dev, 0), HEADDIM)
    step = jax.nn.softplus(steps.astype(f32) + bias)
    blocks = length // SPAN
    step_blocks = step.reshape(blocks, SPAN, heads_dev)
    cum = jnp.cumsum((rate * step).reshape(blocks, SPAN, heads_dev), axis=1)
    tri = lax.broadcasted_iota(jnp.int32, (SPAN, SPAN), 0) >= lax.broadcasted_iota(
        jnp.int32, (SPAN, SPAN), 1
    )

    first = arrived[0]
    act0 = convolve(
        first,
        jnp.concatenate([bc_taps, x_taps[:, :part]], 1),
        jnp.concatenate([bc_bias, x_bias[:part]], 0),
    )
    b_blocks = act0[:, :STATE].reshape(blocks, SPAN, STATE)
    c_blocks = act0[:, STATE : 2 * STATE].reshape(blocks, SPAN, STATE)

    def local_block(state, inputs):
        x_now, b_now, c_now, step_now, cum_now, skip_now = inputs
        heads_now = step_now.shape[1]
        gram = jnp.dot(c_now, b_now.T, preferred_element_type=f32)
        cum_t = cum_now.T
        decay = jnp.exp(jnp.where(tri[None], cum_t[:, :, None] - cum_t[:, None, :], -jnp.inf))
        mix = (gram[None] * decay * step_now.T[:, None, :]).astype(jnp.bfloat16)
        x_heads = x_now.reshape(SPAN, heads_now, HEADDIM)
        y_block = jnp.einsum("hts,shp->thp", mix, x_heads, preferred_element_type=f32).reshape(
            SPAN, heads_now * HEADDIM
        )
        grown = jnp.repeat(jnp.exp(cum_now), HEADDIM, axis=1)
        y_state = grown * jnp.dot(
            c_now.astype(f32), state, precision=lax.Precision.HIGHEST, preferred_element_type=f32
        )
        y_now = y_block + y_state + skip_now * x_now.astype(f32)
        weight = jnp.exp(cum_now[-1][None, :] - cum_now) * step_now
        xw = (x_heads.astype(f32) * weight[:, :, None]).astype(jnp.bfloat16)
        xw = xw.reshape(SPAN, heads_now * HEADDIM)
        contrib = jnp.einsum("sn,sc->nc", b_now, xw, preferred_element_type=f32)
        fade = jnp.exp(jnp.repeat(cum_now[-1], HEADDIM))
        return (state * fade[None, :] + contrib, y_now)

    finals, ys = [], []
    for c in range(CHUNKS):
        lo, hi = c * part, (c + 1) * part
        if c == 0:
            x_act = act0[:, 2 * STATE :]
        else:
            x_act = convolve(arrived[c], x_taps[:, lo:hi], x_bias[lo:hi])
        hs = slice(c * part_heads, (c + 1) * part_heads)
        skip_c = jnp.broadcast_to(skip[lo:hi], (blocks, part))
        final, y_blocks = lax.scan(
            local_block,
            jnp.zeros((STATE, part), f32),
            (
                x_act.reshape(blocks, SPAN, part),
                b_blocks,
                c_blocks,
                step_blocks[:, :, hs],
                cum[:, :, hs],
                skip_c,
            ),
        )
        finals.append(final)
        ys.append(y_blocks)
    final = jnp.concatenate(finals, 1)
    y_blocks = jnp.concatenate(ys, 2)

    block_totals = cum[:, -1, :]
    totals = jnp.sum(block_totals, axis=0)
    tail = jnp.broadcast_to(jnp.repeat(totals, HEADDIM)[None, :], (8, slab))
    gathered = lax.all_gather(jnp.concatenate([final, tail], 0), "ctx")
    shards = gathered.shape[0]
    position = lax.axis_index("ctx")
    finals = gathered[:, :STATE]
    shard_totals = gathered[:, STATE]
    before_shard = jnp.cumsum(shard_totals, axis=0) - shard_totals
    reach = jnp.sum(jnp.where(jnp.arange(shards)[:, None] < position, shard_totals, 0.0), axis=0)
    after_own = before_shard + shard_totals
    live = jnp.arange(shards)[:, None] < position
    weights = jnp.where(live, jnp.exp(jnp.where(live, reach[None] - after_own, 0.0)), 0.0)
    incoming = jnp.sum(weights[:, None, :] * finals, axis=0)
    before = jnp.concatenate(
        [jnp.zeros((1, heads_dev), f32), jnp.cumsum(block_totals, axis=0)[:-1]], 0
    )
    lifted = jnp.exp(jnp.repeat(cum + before[:, None, :], HEADDIM, axis=2))
    y_in = lifted * jnp.einsum(
        "bqn,nc->bqc", c_blocks.astype(f32), incoming, precision=lax.Precision.HIGHEST
    )
    result = y_blocks + y_in
    return result.astype(jnp.bfloat16).reshape(length, slab)


def solution(mesh):
    placed = (P(("ctx", "head"), None), P(("ctx", "head"), None), P(), P(), P(), P(), P())
    return jax.shard_map(
        on_device, mesh=mesh, in_specs=placed, out_specs=P("ctx", "head"), check_vma=False
    )
```

```python
import jax
import jax.numpy as jnp
from jax import lax
from jax.sharding import PartitionSpec as P

HEADS = 256
HEADDIM = 64
STATE = 256
GROUPS = 8
CONV = 4
SPAN = 512
CHUNKS = 4


def shifted(value, axis, by):
    size = lax.axis_size(axis)
    pairs = [(i, i + by) for i in range(size) if 0 <= i + by < size]
    return lax.ppermute(value, axis, pairs)


def convolve(local, kernel, offset):
    length = local.shape[0]
    rim = shifted(local[length - (CONV - 1) :], "ctx", 1)
    padded = jnp.concatenate([rim, local], 0)
    total = padded[0:length].astype(jnp.float32) * kernel[0]
    for k in range(1, CONV):
        total = total + padded[k : k + length].astype(jnp.float32) * kernel[k]
    return jax.nn.silu(total + offset).astype(jnp.bfloat16)


def on_device(conv_input, dt_raw, conv_weight, conv_bias, a_log, dt_bias, d_skip):
    f32 = jnp.float32
    head_count = lax.axis_size("head")
    heads_dev = HEADS // head_count
    repeat_count = head_count // GROUPS
    head_pos = lax.axis_index("head")
    group = head_pos // repeat_count
    rows = conv_input.shape[0]
    x_width = HEADS * HEADDIM
    slab = heads_dev * HEADDIM
    part_heads = heads_dev // CHUNKS
    part = part_heads * HEADDIM
    x_part = conv_input[:, :x_width].reshape(rows, head_count, slab)
    bc = conv_input[:, x_width:].reshape(rows, 2, GROUPS, STATE)
    b_part = jnp.repeat(bc[:, 0], repeat_count, axis=1)
    c_part = jnp.repeat(bc[:, 1], repeat_count, axis=1)
    step_part = dt_raw.reshape(rows, head_count, heads_dev)
    steps = lax.all_to_all(step_part, "head", split_axis=1, concat_axis=0, tiled=True)
    length = steps.shape[0]
    steps = steps.reshape(length, heads_dev)
    sends = [jnp.concatenate([b_part, c_part, x_part[:, :, :part]], axis=2)]
    for c in range(1, CHUNKS):
        sends.append(x_part[:, :, c * part : (c + 1) * part])
    arrived = []
    for s in sends:
        if arrived:
            s, _ = lax.optimization_barrier((s, arrived[-1]))
        got = lax.all_to_all(s, "head", split_axis=1, concat_axis=0, tiled=True)
        arrived.append(got.reshape(length, -1))

    taps = conv_weight.astype(f32)
    x_taps = lax.dynamic_slice_in_dim(taps, head_pos * slab, slab, 1)
    x_bias = lax.dynamic_slice_in_dim(conv_bias, head_pos * slab, slab, 0)
    bc_taps = jnp.concatenate(
        [
            lax.dynamic_slice_in_dim(taps, x_width + group * STATE, STATE, 1),
            lax.dynamic_slice_in_dim(taps, x_width + (GROUPS + group) * STATE, STATE, 1),
        ],
        1,
    )
    bc_bias = jnp.concatenate(
        [
            lax.dynamic_slice_in_dim(conv_bias, x_width + group * STATE, STATE, 0),
            lax.dynamic_slice_in_dim(conv_bias, x_width + (GROUPS + group) * STATE, STATE, 0),
        ],
        0,
    )
    rate = -jnp.exp(lax.dynamic_slice_in_dim(a_log, head_pos * heads_dev, heads_dev, 0))
    bias = lax.dynamic_slice_in_dim(dt_bias, head_pos * heads_dev, heads_dev, 0)
    skip = jnp.repeat(lax.dynamic_slice_in_dim(d_skip, head_pos * heads_dev, heads_dev, 0), HEADDIM)
    step = jax.nn.softplus(steps.astype(f32) + bias)
    blocks = length // SPAN
    step_blocks = step.reshape(blocks, SPAN, heads_dev)
    cum = jnp.cumsum((rate * step).reshape(blocks, SPAN, heads_dev), axis=1)
    tri = lax.broadcasted_iota(jnp.int32, (SPAN, SPAN), 0) >= lax.broadcasted_iota(
        jnp.int32, (SPAN, SPAN), 1
    )

    first = arrived[0]
    act0 = convolve(
        first,
        jnp.concatenate([bc_taps, x_taps[:, :part]], 1),
        jnp.concatenate([bc_bias, x_bias[:part]], 0),
    )
    b_blocks = act0[:, :STATE].reshape(blocks, SPAN, STATE)
    c_blocks = act0[:, STATE : 2 * STATE].reshape(blocks, SPAN, STATE)

    grams = jnp.einsum("bqn,bsn->bqs", c_blocks, b_blocks, preferred_element_type=f32)

    def local_block(state, inputs):
        x_now, b_now, gram, step_now, cum_now, skip_now = inputs
        heads_now = step_now.shape[1]
        cum_t = cum_now.T
        decay = jnp.exp(jnp.where(tri[None], cum_t[:, :, None] - cum_t[:, None, :], -jnp.inf))
        mix = (gram[None] * decay * step_now.T[:, None, :]).astype(jnp.bfloat16)
        x_heads = x_now.reshape(SPAN, heads_now, HEADDIM)
        y_block = jnp.einsum("hts,shp->thp", mix, x_heads, preferred_element_type=f32).reshape(
            SPAN, heads_now * HEADDIM
        )
        y_now = y_block + skip_now * x_now.astype(f32)
        weight = jnp.exp(cum_now[-1][None, :] - cum_now) * step_now
        xw = (x_heads.astype(f32) * weight[:, :, None]).astype(jnp.bfloat16)
        xw = xw.reshape(SPAN, heads_now * HEADDIM)
        contrib = jnp.einsum("sn,sc->nc", b_now, xw, preferred_element_type=f32)
        fade = jnp.exp(jnp.repeat(cum_now[-1], HEADDIM))
        return (state * fade[None, :] + contrib, (y_now, state))

    finals, ys, states = [], [], []
    for c in range(CHUNKS):
        lo, hi = c * part, (c + 1) * part
        if c == 0:
            x_act = act0[:, 2 * STATE :]
        else:
            x_act = convolve(arrived[c], x_taps[:, lo:hi], x_bias[lo:hi])
        hs = slice(c * part_heads, (c + 1) * part_heads)
        skip_c = jnp.broadcast_to(skip[lo:hi], (blocks, part))
        final, (y_blocks, entering) = lax.scan(
            local_block,
            jnp.zeros((STATE, part), f32),
            (
                x_act.reshape(blocks, SPAN, part),
                b_blocks,
                grams,
                step_blocks[:, :, hs],
                cum[:, :, hs],
                skip_c,
            ),
        )
        finals.append(final)
        ys.append(y_blocks)
        states.append(entering)
    final = jnp.concatenate(finals, 1)
    y_blocks = jnp.concatenate(ys, 2)
    entering = jnp.concatenate(states, 2)

    block_totals = cum[:, -1, :]
    totals = jnp.sum(block_totals, axis=0)
    tail = jnp.broadcast_to(jnp.repeat(totals, HEADDIM)[None, :], (8, slab))
    gathered = lax.all_gather(jnp.concatenate([final, tail], 0), "ctx")
    shards = gathered.shape[0]
    position = lax.axis_index("ctx")
    finals = gathered[:, :STATE]
    shard_totals = gathered[:, STATE]
    before_shard = jnp.cumsum(shard_totals, axis=0) - shard_totals
    reach = jnp.sum(jnp.where(jnp.arange(shards)[:, None] < position, shard_totals, 0.0), axis=0)
    after_own = before_shard + shard_totals
    live = jnp.arange(shards)[:, None] < position
    weights = jnp.where(live, jnp.exp(jnp.where(live, reach[None] - after_own, 0.0)), 0.0)
    incoming = jnp.sum(weights[:, None, :] * finals, axis=0)
    before = jnp.concatenate(
        [jnp.zeros((1, heads_dev), f32), jnp.cumsum(block_totals, axis=0)[:-1]], 0
    )
    carried = jnp.exp(jnp.repeat(before, HEADDIM, axis=1))[:, None, :] * incoming[None]
    full_state = entering + carried
    grown = jnp.exp(jnp.repeat(cum, HEADDIM, axis=2))
    y_state = grown * jnp.einsum(
        "bqn,bnc->bqc", c_blocks.astype(f32), full_state, precision=lax.Precision.HIGHEST
    )
    result = y_blocks + y_state
    return result.astype(jnp.bfloat16).reshape(length, slab)


def solution(mesh):
    placed = (P(("ctx", "head"), None), P(("ctx", "head"), None), P(), P(), P(), P(), P())
    return jax.shard_map(
        on_device, mesh=mesh, in_specs=placed, out_specs=P("ctx", "head"), check_vma=False
    )
```

```python
import jax
import jax.numpy as jnp
from jax import lax
from jax.sharding import PartitionSpec as P

HEADS = 256
HEADDIM = 64
STATE = 256
GROUPS = 8
CONV = 4
SPAN = 512


def on_device(conv_input, dt_raw, conv_weight, conv_bias, a_log, dt_bias, d_skip):
    f32 = jnp.float32
    head_count = lax.axis_size("head")
    ctx_count = lax.axis_size("ctx")
    heads_dev = HEADS // head_count
    repeat_count = head_count // GROUPS
    head_pos = lax.axis_index("head")
    rows = conv_input.shape[0]
    x_width = HEADS * HEADDIM
    slab = heads_dev * HEADDIM
    devices = ctx_count * head_count
    rim = lax.ppermute(
        conv_input[rows - (CONV - 1) :], ("ctx", "head"), [(i, i + 1) for i in range(devices - 1)]
    )
    padded = jnp.concatenate([rim, conv_input], 0)
    taps = conv_weight.astype(f32)
    total = padded[0:rows].astype(f32) * taps[0]
    for k in range(1, CONV):
        total = total + padded[k : k + rows].astype(f32) * taps[k]
    act = jax.nn.silu(total + conv_bias).astype(jnp.bfloat16)

    def payload(target):
        group = target // repeat_count
        return jnp.concatenate(
            [
                lax.dynamic_slice_in_dim(act, target * slab, slab, 1),
                lax.dynamic_slice_in_dim(act, x_width + group * STATE, STATE, 1),
                lax.dynamic_slice_in_dim(act, x_width + (GROUPS + group) * STATE, STATE, 1),
                lax.dynamic_slice_in_dim(dt_raw, target * heads_dev, heads_dev, 1),
            ],
            1,
        )

    rate = -jnp.exp(lax.dynamic_slice_in_dim(a_log, head_pos * heads_dev, heads_dev, 0))
    bias = lax.dynamic_slice_in_dim(dt_bias, head_pos * heads_dev, heads_dev, 0)
    skip = jnp.repeat(lax.dynamic_slice_in_dim(d_skip, head_pos * heads_dev, heads_dev, 0), HEADDIM)
    tri = lax.broadcasted_iota(jnp.int32, (SPAN, SPAN), 0) >= lax.broadcasted_iota(
        jnp.int32, (SPAN, SPAN), 1
    )
    pairs = head_count // 2
    blocks = pairs
    parity = head_pos % 2
    y_acc = jnp.zeros((blocks, SPAN, slab), f32)
    c_acc = jnp.zeros((blocks, SPAN, STATE), jnp.bfloat16)
    cum_acc = jnp.zeros((blocks, SPAN, heads_dev), f32)
    contrib_acc = jnp.zeros((blocks, STATE, slab), f32)
    done = []
    rings = 4
    across = pairs // rings
    order = [(0, 0), (1, 0), (rings - 1, 0)] + [(d, 1) for d in (0, 1, rings - 1)]
    order = order + [(2, 0), (2, 1)]

    def moved(p, dz, dx):
        return ((p // across + dz) % rings) * across + (p % across + dx) % across

    for m, (dz, dx) in enumerate(order):
        same = [(i, 2 * moved(i // 2, dz, dx) + i % 2) for i in range(head_count)]
        other = [(i, 2 * moved(i // 2, dz, dx) + 1 - i % 2) for i in range(head_count)]
        t_same = 2 * moved(head_pos // 2, dz, dx) + parity
        t_other = 2 * moved(head_pos // 2, dz, dx) + 1 - parity
        p_same, p_other = payload(t_same), payload(t_other)
        if m >= 2:
            p_same, p_other, _ = lax.optimization_barrier((p_same, p_other, done[m - 2]))
        r_same = lax.ppermute(p_same, "head", same)
        r_other = lax.ppermute(p_other, "head", other)
        first = jnp.where(parity == 0, r_same, r_other)
        second = jnp.where(parity == 0, r_other, r_same)
        blk = jnp.concatenate([first, second], 0)
        k = moved(head_pos // 2, rings - dz, across - dx)
        x_now = blk[:, :slab]
        b_now = blk[:, slab : slab + STATE]
        c_now = blk[:, slab + STATE : slab + 2 * STATE]
        step_now = jax.nn.softplus(blk[:, slab + 2 * STATE :].astype(f32) + bias)
        cum_now = jnp.cumsum(rate * step_now, axis=0)
        gram = jnp.dot(c_now, b_now.T, preferred_element_type=f32)
        cum_t = cum_now.T
        decay = jnp.exp(jnp.where(tri[None], cum_t[:, :, None] - cum_t[:, None, :], -jnp.inf))
        mix = (gram[None] * decay * step_now.T[:, None, :]).astype(jnp.bfloat16)
        x_heads = x_now.reshape(SPAN, heads_dev, HEADDIM)
        y_block = jnp.einsum("hts,shp->thp", mix, x_heads, preferred_element_type=f32).reshape(
            SPAN, slab
        )
        y_now = y_block + skip * x_now.astype(f32)
        weight = jnp.exp(cum_now[-1][None, :] - cum_now) * step_now
        xw = (x_heads.astype(f32) * weight[:, :, None]).astype(jnp.bfloat16).reshape(SPAN, slab)
        contrib = jnp.einsum("sn,sc->nc", b_now, xw, preferred_element_type=f32)
        y_acc = lax.dynamic_update_index_in_dim(y_acc, y_now, k, 0)
        c_acc = lax.dynamic_update_index_in_dim(c_acc, c_now, k, 0)
        cum_acc = lax.dynamic_update_index_in_dim(cum_acc, cum_now, k, 0)
        contrib_acc = lax.dynamic_update_index_in_dim(contrib_acc, contrib, k, 0)
        done.append((contrib, y_now))

    block_totals = cum_acc[:, -1, :]
    state = jnp.zeros((STATE, slab), f32)
    entering = []
    for k in range(blocks):
        entering.append(state)
        fade = jnp.exp(jnp.repeat(block_totals[k], HEADDIM))
        state = state * fade[None, :] + contrib_acc[k]
    final = state
    entering = jnp.stack(entering)
    totals = jnp.sum(block_totals, axis=0)
    tail = jnp.broadcast_to(jnp.repeat(totals, HEADDIM)[None, :], (8, slab))
    gathered = lax.all_gather(jnp.concatenate([final, tail], 0), "ctx")
    shards = gathered.shape[0]
    position = lax.axis_index("ctx")
    finals = gathered[:, :STATE]
    shard_totals = gathered[:, STATE]
    before_shard = jnp.cumsum(shard_totals, axis=0) - shard_totals
    reach = jnp.sum(jnp.where(jnp.arange(shards)[:, None] < position, shard_totals, 0.0), axis=0)
    after_own = before_shard + shard_totals
    live = jnp.arange(shards)[:, None] < position
    weights = jnp.where(live, jnp.exp(jnp.where(live, reach[None] - after_own, 0.0)), 0.0)
    incoming = jnp.sum(weights[:, None, :] * finals, axis=0)
    before = jnp.concatenate(
        [jnp.zeros((1, heads_dev), f32), jnp.cumsum(block_totals, axis=0)[:-1]], 0
    )
    carried = jnp.exp(jnp.repeat(before, HEADDIM, axis=1))[:, None, :] * incoming[None]
    full_state = entering + carried
    grown = jnp.exp(jnp.repeat(cum_acc, HEADDIM, axis=2))
    y_state = grown * jnp.einsum(
        "bqn,bnc->bqc", c_acc.astype(f32), full_state, precision=lax.Precision.HIGHEST
    )
    result = y_acc + y_state
    return result.astype(jnp.bfloat16).reshape(blocks * SPAN, slab)


def solution(mesh):
    placed = (P(("ctx", "head"), None), P(("ctx", "head"), None), P(), P(), P(), P(), P())
    return jax.shard_map(
        on_device, mesh=mesh, in_specs=placed, out_specs=P("ctx", "head"), check_vma=False
    )
```

```python
import jax
import jax.numpy as jnp
from jax import lax
from jax.sharding import PartitionSpec as P

HEADS = 256
HEADDIM = 64
STATE = 256
GROUPS = 8
CONV = 4
SPAN = 512


def on_device(conv_input, dt_raw, conv_weight, conv_bias, a_log, dt_bias, d_skip):
    f32 = jnp.float32
    head_count = lax.axis_size("head")
    ctx_count = lax.axis_size("ctx")
    heads_dev = HEADS // head_count
    repeat_count = head_count // GROUPS
    head_pos = lax.axis_index("head")
    rows = conv_input.shape[0]
    x_width = HEADS * HEADDIM
    slab = heads_dev * HEADDIM
    devices = ctx_count * head_count
    rim = lax.ppermute(
        conv_input[rows - (CONV - 1) :], ("ctx", "head"), [(i, i + 1) for i in range(devices - 1)]
    )
    padded = jnp.concatenate([rim, conv_input], 0)
    taps = conv_weight.astype(f32)

    def payload(target):
        group = target // repeat_count

        def pick(table):
            last = table.ndim - 1
            return jnp.concatenate(
                [
                    lax.dynamic_slice_in_dim(table, target * slab, slab, last),
                    lax.dynamic_slice_in_dim(table, x_width + group * STATE, STATE, last),
                    lax.dynamic_slice_in_dim(
                        table, x_width + (GROUPS + group) * STATE, STATE, last
                    ),
                ],
                last,
            )

        window, kernel = pick(padded), pick(taps)
        total = window[0:rows].astype(f32) * kernel[0]
        for k in range(1, CONV):
            total = total + window[k : k + rows].astype(f32) * kernel[k]
        act = jax.nn.silu(total + pick(conv_bias)).astype(jnp.bfloat16)
        steps = lax.dynamic_slice_in_dim(dt_raw, target * heads_dev, heads_dev, 1)
        return jnp.concatenate([act, steps], 1)

    rate = -jnp.exp(lax.dynamic_slice_in_dim(a_log, head_pos * heads_dev, heads_dev, 0))
    bias = lax.dynamic_slice_in_dim(dt_bias, head_pos * heads_dev, heads_dev, 0)
    skip = jnp.repeat(lax.dynamic_slice_in_dim(d_skip, head_pos * heads_dev, heads_dev, 0), HEADDIM)
    tri = lax.broadcasted_iota(jnp.int32, (SPAN, SPAN), 0) >= lax.broadcasted_iota(
        jnp.int32, (SPAN, SPAN), 1
    )
    pairs = head_count // 2
    blocks = pairs
    parity = head_pos % 2
    y_acc = jnp.zeros((blocks, SPAN, slab), f32)
    c_acc = jnp.zeros((blocks, SPAN, STATE), jnp.bfloat16)
    cum_acc = jnp.zeros((blocks, SPAN, heads_dev), f32)
    contrib_acc = jnp.zeros((blocks, STATE, slab), f32)
    done = []
    for m in range(blocks):
        same = [(i, 2 * ((i // 2 + m) % pairs) + i % 2) for i in range(head_count)]
        other = [(i, 2 * ((i // 2 + m) % pairs) + 1 - i % 2) for i in range(head_count)]
        t_same = 2 * ((head_pos // 2 + m) % pairs) + parity
        t_other = 2 * ((head_pos // 2 + m) % pairs) + 1 - parity
        p_same, p_other = payload(t_same), payload(t_other)
        if m >= 2:
            p_same, p_other, _ = lax.optimization_barrier((p_same, p_other, done[m - 2]))
        r_same = lax.ppermute(p_same, "head", same)
        r_other = lax.ppermute(p_other, "head", other)
        first = jnp.where(parity == 0, r_same, r_other)
        second = jnp.where(parity == 0, r_other, r_same)
        blk = jnp.concatenate([first, second], 0)
        k = (head_pos // 2 - m) % pairs
        x_now = blk[:, :slab]
        b_now = blk[:, slab : slab + STATE]
        c_now = blk[:, slab + STATE : slab + 2 * STATE]
        step_now = jax.nn.softplus(blk[:, slab + 2 * STATE :].astype(f32) + bias)
        cum_now = jnp.cumsum(rate * step_now, axis=0)
        gram = jnp.dot(c_now, b_now.T, preferred_element_type=f32)
        cum_t = cum_now.T
        decay = jnp.exp(jnp.where(tri[None], cum_t[:, :, None] - cum_t[:, None, :], -jnp.inf))
        mix = (gram[None] * decay * step_now.T[:, None, :]).astype(jnp.bfloat16)
        x_heads = x_now.reshape(SPAN, heads_dev, HEADDIM)
        y_block = jnp.einsum("hts,shp->thp", mix, x_heads, preferred_element_type=f32).reshape(
            SPAN, slab
        )
        y_now = y_block + skip * x_now.astype(f32)
        weight = jnp.exp(cum_now[-1][None, :] - cum_now) * step_now
        xw = (x_heads.astype(f32) * weight[:, :, None]).astype(jnp.bfloat16).reshape(SPAN, slab)
        contrib = jnp.einsum("sn,sc->nc", b_now, xw, preferred_element_type=f32)
        y_acc = lax.dynamic_update_index_in_dim(y_acc, y_now, k, 0)
        c_acc = lax.dynamic_update_index_in_dim(c_acc, c_now, k, 0)
        cum_acc = lax.dynamic_update_index_in_dim(cum_acc, cum_now, k, 0)
        contrib_acc = lax.dynamic_update_index_in_dim(contrib_acc, contrib, k, 0)
        done.append((contrib, y_now))

    block_totals = cum_acc[:, -1, :]
    state = jnp.zeros((STATE, slab), f32)
    entering = []
    for k in range(blocks):
        entering.append(state)
        fade = jnp.exp(jnp.repeat(block_totals[k], HEADDIM))
        state = state * fade[None, :] + contrib_acc[k]
    final = state
    entering = jnp.stack(entering)
    totals = jnp.sum(block_totals, axis=0)
    tail = jnp.broadcast_to(jnp.repeat(totals, HEADDIM)[None, :], (8, slab))
    gathered = lax.all_gather(jnp.concatenate([final, tail], 0), "ctx")
    shards = gathered.shape[0]
    position = lax.axis_index("ctx")
    finals = gathered[:, :STATE]
    shard_totals = gathered[:, STATE]
    before_shard = jnp.cumsum(shard_totals, axis=0) - shard_totals
    reach = jnp.sum(jnp.where(jnp.arange(shards)[:, None] < position, shard_totals, 0.0), axis=0)
    after_own = before_shard + shard_totals
    live = jnp.arange(shards)[:, None] < position
    weights = jnp.where(live, jnp.exp(jnp.where(live, reach[None] - after_own, 0.0)), 0.0)
    incoming = jnp.sum(weights[:, None, :] * finals, axis=0)
    before = jnp.concatenate(
        [jnp.zeros((1, heads_dev), f32), jnp.cumsum(block_totals, axis=0)[:-1]], 0
    )
    carried = jnp.exp(jnp.repeat(before, HEADDIM, axis=1))[:, None, :] * incoming[None]
    full_state = entering + carried
    grown = jnp.exp(jnp.repeat(cum_acc, HEADDIM, axis=2))
    y_state = grown * jnp.einsum(
        "bqn,bnc->bqc", c_acc.astype(f32), full_state, precision=lax.Precision.HIGHEST
    )
    result = y_acc + y_state
    return result.astype(jnp.bfloat16).reshape(blocks * SPAN, slab)


def solution(mesh):
    placed = (P(("ctx", "head"), None), P(("ctx", "head"), None), P(), P(), P(), P(), P())
    return jax.shard_map(
        on_device, mesh=mesh, in_specs=placed, out_specs=P("ctx", "head"), check_vma=False
    )
```

```python
import jax
import jax.numpy as jnp
from jax import lax
from jax.sharding import PartitionSpec as P

HEADS = 256
HEADDIM = 64
STATE = 256
GROUPS = 8
CONV = 4
SPAN = 512


def on_device(conv_input, dt_raw, conv_weight, conv_bias, a_log, dt_bias, d_skip):
    f32 = jnp.float32
    head_count = lax.axis_size("head")
    ctx_count = lax.axis_size("ctx")
    heads_dev = HEADS // head_count
    repeat_count = head_count // GROUPS
    head_pos = lax.axis_index("head")
    rows = conv_input.shape[0]
    x_width = HEADS * HEADDIM
    slab = heads_dev * HEADDIM
    devices = ctx_count * head_count
    rim = lax.ppermute(
        conv_input[rows - (CONV - 1) :], ("ctx", "head"), [(i, i + 1) for i in range(devices - 1)]
    )
    padded = jnp.concatenate([rim, conv_input], 0)
    taps = conv_weight.astype(f32)
    total = padded[0:rows].astype(f32) * taps[0]
    for k in range(1, CONV):
        total = total + padded[k : k + rows].astype(f32) * taps[k]
    act = jax.nn.silu(total + conv_bias).astype(jnp.bfloat16)

    def payload(target):
        group = target // repeat_count
        return jnp.concatenate(
            [
                lax.dynamic_slice_in_dim(act, target * slab, slab, 1),
                lax.dynamic_slice_in_dim(act, x_width + group * STATE, STATE, 1),
                lax.dynamic_slice_in_dim(act, x_width + (GROUPS + group) * STATE, STATE, 1),
                lax.dynamic_slice_in_dim(dt_raw, target * heads_dev, heads_dev, 1),
            ],
            1,
        )

    rate = -jnp.exp(lax.dynamic_slice_in_dim(a_log, head_pos * heads_dev, heads_dev, 0))
    bias = lax.dynamic_slice_in_dim(dt_bias, head_pos * heads_dev, heads_dev, 0)
    skip = jnp.repeat(lax.dynamic_slice_in_dim(d_skip, head_pos * heads_dev, heads_dev, 0), HEADDIM)
    tri = lax.broadcasted_iota(jnp.int32, (SPAN, SPAN), 0) >= lax.broadcasted_iota(
        jnp.int32, (SPAN, SPAN), 1
    )
    pairs = head_count // 2
    blocks = pairs
    parity = head_pos % 2
    y_acc = jnp.zeros((blocks, SPAN, slab), f32)
    c_acc = jnp.zeros((blocks, SPAN, STATE), jnp.bfloat16)
    cum_acc = jnp.zeros((blocks, SPAN, heads_dev), f32)
    contrib_acc = jnp.zeros((blocks, STATE, slab), f32)
    done = []
    for m in range(blocks):
        same = [(i, 2 * ((i // 2 + m) % pairs) + i % 2) for i in range(head_count)]
        other = [(i, 2 * ((i // 2 + m) % pairs) + 1 - i % 2) for i in range(head_count)]
        t_same = 2 * ((head_pos // 2 + m) % pairs) + parity
        t_other = 2 * ((head_pos // 2 + m) % pairs) + 1 - parity
        p_same, p_other = payload(t_same), payload(t_other)
        if m >= 4:
            p_same, p_other, _ = lax.optimization_barrier((p_same, p_other, done[m - 4]))
        r_same = lax.ppermute(p_same, "head", same)
        r_other = lax.ppermute(p_other, "head", other)
        first = jnp.where(parity == 0, r_same, r_other)
        second = jnp.where(parity == 0, r_other, r_same)
        blk = jnp.concatenate([first, second], 0)
        k = (head_pos // 2 - m) % pairs
        x_now = blk[:, :slab]
        b_now = blk[:, slab : slab + STATE]
        c_now = blk[:, slab + STATE : slab + 2 * STATE]
        step_now = jax.nn.softplus(blk[:, slab + 2 * STATE :].astype(f32) + bias)
        cum_now = jnp.cumsum(rate * step_now, axis=0)
        gram = jnp.dot(c_now, b_now.T, preferred_element_type=f32)
        cum_t = cum_now.T
        decay = jnp.exp(jnp.where(tri[None], cum_t[:, :, None] - cum_t[:, None, :], -jnp.inf))
        mix = (gram[None] * decay * step_now.T[:, None, :]).astype(jnp.bfloat16)
        x_heads = x_now.reshape(SPAN, heads_dev, HEADDIM)
        y_block = jnp.einsum("hts,shp->thp", mix, x_heads, preferred_element_type=f32).reshape(
            SPAN, slab
        )
        y_now = y_block + skip * x_now.astype(f32)
        weight = jnp.exp(cum_now[-1][None, :] - cum_now) * step_now
        xw = (x_heads.astype(f32) * weight[:, :, None]).astype(jnp.bfloat16).reshape(SPAN, slab)
        contrib = jnp.einsum("sn,sc->nc", b_now, xw, preferred_element_type=f32)
        y_acc = lax.dynamic_update_index_in_dim(y_acc, y_now, k, 0)
        c_acc = lax.dynamic_update_index_in_dim(c_acc, c_now, k, 0)
        cum_acc = lax.dynamic_update_index_in_dim(cum_acc, cum_now, k, 0)
        contrib_acc = lax.dynamic_update_index_in_dim(contrib_acc, contrib, k, 0)
        done.append((contrib, y_now))

    block_totals = cum_acc[:, -1, :]
    state = jnp.zeros((STATE, slab), f32)
    entering = []
    for k in range(blocks):
        entering.append(state)
        fade = jnp.exp(jnp.repeat(block_totals[k], HEADDIM))
        state = state * fade[None, :] + contrib_acc[k]
    final = state
    entering = jnp.stack(entering)
    totals = jnp.sum(block_totals, axis=0)
    tail = jnp.broadcast_to(jnp.repeat(totals, HEADDIM)[None, :], (8, slab))
    gathered = lax.all_gather(jnp.concatenate([final, tail], 0), "ctx")
    shards = gathered.shape[0]
    position = lax.axis_index("ctx")
    finals = gathered[:, :STATE]
    shard_totals = gathered[:, STATE]
    before_shard = jnp.cumsum(shard_totals, axis=0) - shard_totals
    reach = jnp.sum(jnp.where(jnp.arange(shards)[:, None] < position, shard_totals, 0.0), axis=0)
    after_own = before_shard + shard_totals
    live = jnp.arange(shards)[:, None] < position
    weights = jnp.where(live, jnp.exp(jnp.where(live, reach[None] - after_own, 0.0)), 0.0)
    incoming = jnp.sum(weights[:, None, :] * finals, axis=0)
    before = jnp.concatenate(
        [jnp.zeros((1, heads_dev), f32), jnp.cumsum(block_totals, axis=0)[:-1]], 0
    )
    carried = jnp.exp(jnp.repeat(before, HEADDIM, axis=1))[:, None, :] * incoming[None]
    full_state = entering + carried
    grown = jnp.exp(jnp.repeat(cum_acc, HEADDIM, axis=2))
    y_state = grown * jnp.einsum(
        "bqn,bnc->bqc", c_acc.astype(f32), full_state, precision=lax.Precision.HIGHEST
    )
    result = y_acc + y_state
    return result.astype(jnp.bfloat16).reshape(blocks * SPAN, slab)


def solution(mesh):
    placed = (P(("ctx", "head"), None), P(("ctx", "head"), None), P(), P(), P(), P(), P())
    return jax.shard_map(
        on_device, mesh=mesh, in_specs=placed, out_specs=P("ctx", "head"), check_vma=False
    )
```

```python
import jax
import jax.numpy as jnp
from jax import lax
from jax.sharding import PartitionSpec as P

HEADS = 256
HEADDIM = 64
STATE = 256
GROUPS = 8
CONV = 4
SPAN = 512


def on_device(conv_input, dt_raw, conv_weight, conv_bias, a_log, dt_bias, d_skip):
    f32 = jnp.float32
    head_count = lax.axis_size("head")
    ctx_count = lax.axis_size("ctx")
    heads_dev = HEADS // head_count
    repeat_count = head_count // GROUPS
    head_pos = lax.axis_index("head")
    rows = conv_input.shape[0]
    x_width = HEADS * HEADDIM
    slab = heads_dev * HEADDIM
    devices = ctx_count * head_count
    rim = lax.ppermute(
        conv_input[rows - (CONV - 1) :], ("ctx", "head"), [(i, i + 1) for i in range(devices - 1)]
    )
    padded = jnp.concatenate([rim, conv_input], 0)
    taps = conv_weight.astype(f32)
    total = padded[0:rows].astype(f32) * taps[0]
    for k in range(1, CONV):
        total = total + padded[k : k + rows].astype(f32) * taps[k]
    act = jax.nn.silu(total + conv_bias).astype(jnp.bfloat16)

    def payload(target):
        group = target // repeat_count
        return jnp.concatenate(
            [
                lax.dynamic_slice_in_dim(act, target * slab, slab, 1),
                lax.dynamic_slice_in_dim(act, x_width + group * STATE, STATE, 1),
                lax.dynamic_slice_in_dim(act, x_width + (GROUPS + group) * STATE, STATE, 1),
                lax.dynamic_slice_in_dim(dt_raw, target * heads_dev, heads_dev, 1),
            ],
            1,
        )

    rate = -jnp.exp(lax.dynamic_slice_in_dim(a_log, head_pos * heads_dev, heads_dev, 0))
    bias = lax.dynamic_slice_in_dim(dt_bias, head_pos * heads_dev, heads_dev, 0)
    skip = jnp.repeat(lax.dynamic_slice_in_dim(d_skip, head_pos * heads_dev, heads_dev, 0), HEADDIM)
    tri = lax.broadcasted_iota(jnp.int32, (SPAN, SPAN), 0) >= lax.broadcasted_iota(
        jnp.int32, (SPAN, SPAN), 1
    )
    pairs = head_count // 2
    blocks = pairs
    parity = head_pos % 2
    y_acc = jnp.zeros((blocks, SPAN, slab), f32)
    c_acc = jnp.zeros((blocks, SPAN, STATE), jnp.bfloat16)
    cum_acc = jnp.zeros((blocks, SPAN, heads_dev), f32)
    contrib_acc = jnp.zeros((blocks, STATE, slab), f32)
    done = []
    for m in range(blocks):
        same = [(i, 2 * ((i // 2 + m) % pairs) + i % 2) for i in range(head_count)]
        other = [(i, 2 * ((i // 2 + m) % pairs) + 1 - i % 2) for i in range(head_count)]
        t_same = 2 * ((head_pos // 2 + m) % pairs) + parity
        t_other = 2 * ((head_pos // 2 + m) % pairs) + 1 - parity
        p_same, p_other = payload(t_same), payload(t_other)
        if m >= 6:
            p_same, p_other, _ = lax.optimization_barrier((p_same, p_other, done[m - 6]))
        r_same = lax.ppermute(p_same, "head", same)
        r_other = lax.ppermute(p_other, "head", other)
        first = jnp.where(parity == 0, r_same, r_other)
        second = jnp.where(parity == 0, r_other, r_same)
        blk = jnp.concatenate([first, second], 0)
        k = (head_pos // 2 - m) % pairs
        x_now = blk[:, :slab]
        b_now = blk[:, slab : slab + STATE]
        c_now = blk[:, slab + STATE : slab + 2 * STATE]
        step_now = jax.nn.softplus(blk[:, slab + 2 * STATE :].astype(f32) + bias)
        cum_now = jnp.cumsum(rate * step_now, axis=0)
        gram = jnp.dot(c_now, b_now.T, preferred_element_type=f32)
        cum_t = cum_now.T
        decay = jnp.exp(jnp.where(tri[None], cum_t[:, :, None] - cum_t[:, None, :], -jnp.inf))
        mix = (gram[None] * decay * step_now.T[:, None, :]).astype(jnp.bfloat16)
        x_heads = x_now.reshape(SPAN, heads_dev, HEADDIM)
        y_block = jnp.einsum("hts,shp->thp", mix, x_heads, preferred_element_type=f32).reshape(
            SPAN, slab
        )
        y_now = y_block + skip * x_now.astype(f32)
        weight = jnp.exp(cum_now[-1][None, :] - cum_now) * step_now
        xw = (x_heads.astype(f32) * weight[:, :, None]).astype(jnp.bfloat16).reshape(SPAN, slab)
        contrib = jnp.einsum("sn,sc->nc", b_now, xw, preferred_element_type=f32)
        y_acc = lax.dynamic_update_index_in_dim(y_acc, y_now, k, 0)
        c_acc = lax.dynamic_update_index_in_dim(c_acc, c_now, k, 0)
        cum_acc = lax.dynamic_update_index_in_dim(cum_acc, cum_now, k, 0)
        contrib_acc = lax.dynamic_update_index_in_dim(contrib_acc, contrib, k, 0)
        done.append((contrib, y_now))

    block_totals = cum_acc[:, -1, :]
    state = jnp.zeros((STATE, slab), f32)
    entering = []
    for k in range(blocks):
        entering.append(state)
        fade = jnp.exp(jnp.repeat(block_totals[k], HEADDIM))
        state = state * fade[None, :] + contrib_acc[k]
    final = state
    entering = jnp.stack(entering)
    totals = jnp.sum(block_totals, axis=0)
    tail = jnp.broadcast_to(jnp.repeat(totals, HEADDIM)[None, :], (8, slab))
    gathered = lax.all_gather(jnp.concatenate([final, tail], 0), "ctx")
    shards = gathered.shape[0]
    position = lax.axis_index("ctx")
    finals = gathered[:, :STATE]
    shard_totals = gathered[:, STATE]
    before_shard = jnp.cumsum(shard_totals, axis=0) - shard_totals
    reach = jnp.sum(jnp.where(jnp.arange(shards)[:, None] < position, shard_totals, 0.0), axis=0)
    after_own = before_shard + shard_totals
    live = jnp.arange(shards)[:, None] < position
    weights = jnp.where(live, jnp.exp(jnp.where(live, reach[None] - after_own, 0.0)), 0.0)
    incoming = jnp.sum(weights[:, None, :] * finals, axis=0)
    before = jnp.concatenate(
        [jnp.zeros((1, heads_dev), f32), jnp.cumsum(block_totals, axis=0)[:-1]], 0
    )
    carried = jnp.exp(jnp.repeat(before, HEADDIM, axis=1))[:, None, :] * incoming[None]
    full_state = entering + carried
    grown = jnp.exp(jnp.repeat(cum_acc, HEADDIM, axis=2))
    y_state = grown * jnp.einsum(
        "bqn,bnc->bqc", c_acc.astype(f32), full_state, precision=lax.Precision.HIGHEST
    )
    result = y_acc + y_state
    return result.astype(jnp.bfloat16).reshape(blocks * SPAN, slab)


def solution(mesh):
    placed = (P(("ctx", "head"), None), P(("ctx", "head"), None), P(), P(), P(), P(), P())
    return jax.shard_map(
        on_device, mesh=mesh, in_specs=placed, out_specs=P("ctx", "head"), check_vma=False
    )
```

```python
import jax
import jax.numpy as jnp
from jax import lax
from jax.sharding import PartitionSpec as P

HEADS = 256
HEADDIM = 64
STATE = 256
GROUPS = 8
CONV = 4
SPAN = 512


def on_device(conv_input, dt_raw, conv_weight, conv_bias, a_log, dt_bias, d_skip):
    f32 = jnp.float32
    head_count = lax.axis_size("head")
    ctx_count = lax.axis_size("ctx")
    heads_dev = HEADS // head_count
    repeat_count = head_count // GROUPS
    head_pos = lax.axis_index("head")
    rows = conv_input.shape[0]
    x_width = HEADS * HEADDIM
    slab = heads_dev * HEADDIM
    devices = ctx_count * head_count
    rim = lax.ppermute(
        conv_input[rows - (CONV - 1) :], ("ctx", "head"), [(i, i + 1) for i in range(devices - 1)]
    )
    padded = jnp.concatenate([rim, conv_input], 0)
    taps = conv_weight.astype(f32)
    total = padded[0:rows].astype(f32) * taps[0]
    for k in range(1, CONV):
        total = total + padded[k : k + rows].astype(f32) * taps[k]
    act = jax.nn.silu(total + conv_bias).astype(jnp.bfloat16)

    def payload(target):
        group = target // repeat_count
        return jnp.concatenate(
            [
                lax.dynamic_slice_in_dim(act, target * slab, slab, 1),
                lax.dynamic_slice_in_dim(act, x_width + group * STATE, STATE, 1),
                lax.dynamic_slice_in_dim(act, x_width + (GROUPS + group) * STATE, STATE, 1),
                lax.dynamic_slice_in_dim(dt_raw, target * heads_dev, heads_dev, 1),
            ],
            1,
        )

    rate = -jnp.exp(lax.dynamic_slice_in_dim(a_log, head_pos * heads_dev, heads_dev, 0))
    bias = lax.dynamic_slice_in_dim(dt_bias, head_pos * heads_dev, heads_dev, 0)
    skip = jnp.repeat(lax.dynamic_slice_in_dim(d_skip, head_pos * heads_dev, heads_dev, 0), HEADDIM)
    tri = lax.broadcasted_iota(jnp.int32, (SPAN, SPAN), 0) >= lax.broadcasted_iota(
        jnp.int32, (SPAN, SPAN), 1
    )
    pairs = head_count // 2
    blocks = pairs
    parity = head_pos % 2
    y_acc = jnp.zeros((blocks, SPAN, slab), f32)
    c_acc = jnp.zeros((blocks, SPAN, STATE), jnp.bfloat16)
    cum_acc = jnp.zeros((blocks, SPAN, heads_dev), f32)
    contrib_acc = jnp.zeros((blocks, STATE, slab), f32)
    done = []
    for m in range(blocks):
        same = [(i, 2 * ((i // 2 + m) % pairs) + i % 2) for i in range(head_count)]
        other = [(i, 2 * ((i // 2 + m) % pairs) + 1 - i % 2) for i in range(head_count)]
        t_same = 2 * ((head_pos // 2 + m) % pairs) + parity
        t_other = 2 * ((head_pos // 2 + m) % pairs) + 1 - parity
        p_same, p_other = payload(t_same), payload(t_other)
        if m >= 4:
            p_same, p_other, _ = lax.optimization_barrier((p_same, p_other, done[m - 4]))
        r_same = lax.ppermute(p_same, "head", same)
        r_other = lax.ppermute(p_other, "head", other)
        first = jnp.where(parity == 0, r_same, r_other)
        second = jnp.where(parity == 0, r_other, r_same)
        blk = jnp.concatenate([first, second], 0)
        k = (head_pos // 2 - m) % pairs
        x_now = blk[:, :slab]
        b_now = blk[:, slab : slab + STATE]
        c_now = blk[:, slab + STATE : slab + 2 * STATE]
        step_now = jax.nn.softplus(blk[:, slab + 2 * STATE :].astype(f32) + bias)
        cum_now = jnp.cumsum(rate * step_now, axis=0)
        gram = jnp.dot(c_now, b_now.T, preferred_element_type=f32)
        cum_t = cum_now.T
        decay = jnp.exp(jnp.where(tri[None], cum_t[:, :, None] - cum_t[:, None, :], -jnp.inf))
        mix = (gram[None] * decay * step_now.T[:, None, :]).astype(jnp.bfloat16)
        x_heads = x_now.reshape(SPAN, heads_dev, HEADDIM)
        y_block = jnp.einsum("hts,shp->thp", mix, x_heads, preferred_element_type=f32).reshape(
            SPAN, slab
        )
        y_now = y_block + skip * x_now.astype(f32)
        weight = jnp.exp(cum_now[-1][None, :] - cum_now) * step_now
        xw = (x_heads.astype(f32) * weight[:, :, None]).astype(jnp.bfloat16).reshape(SPAN, slab)
        contrib = jnp.einsum("sn,sc->nc", b_now, xw, preferred_element_type=f32)
        y_acc = lax.dynamic_update_index_in_dim(y_acc, y_now, k, 0)
        c_acc = lax.dynamic_update_index_in_dim(c_acc, c_now, k, 0)
        cum_acc = lax.dynamic_update_index_in_dim(cum_acc, cum_now, k, 0)
        contrib_acc = lax.dynamic_update_index_in_dim(contrib_acc, contrib, k, 0)
        done.append((contrib, y_now))

    block_totals = cum_acc[:, -1, :]
    state = jnp.zeros((STATE, slab), f32)
    entering = []
    for k in range(blocks):
        entering.append(state)
        fade = jnp.exp(jnp.repeat(block_totals[k], HEADDIM))
        state = state * fade[None, :] + contrib_acc[k]
    final = state
    entering = jnp.stack(entering)
    totals = jnp.sum(block_totals, axis=0)
    tail = jnp.broadcast_to(jnp.repeat(totals, HEADDIM)[None, :], (8, slab))
    gathered = lax.all_gather(jnp.concatenate([final, tail], 0), "ctx")
    shards = gathered.shape[0]
    position = lax.axis_index("ctx")
    finals = gathered[:, :STATE]
    shard_totals = gathered[:, STATE]
    before_shard = jnp.cumsum(shard_totals, axis=0) - shard_totals
    reach = jnp.sum(jnp.where(jnp.arange(shards)[:, None] < position, shard_totals, 0.0), axis=0)
    after_own = before_shard + shard_totals
    live = jnp.arange(shards)[:, None] < position
    weights = jnp.where(live, jnp.exp(jnp.where(live, reach[None] - after_own, 0.0)), 0.0)
    incoming = jnp.sum(weights[:, None, :] * finals, axis=0)
    before = jnp.concatenate(
        [jnp.zeros((1, heads_dev), f32), jnp.cumsum(block_totals, axis=0)[:-1]], 0
    )
    carried = jnp.exp(jnp.repeat(before, HEADDIM, axis=1))[:, None, :] * incoming[None]
    full_state = entering + carried
    y_state = jnp.einsum(
        "bqn,bnc->bqc", c_acc.astype(f32), full_state, precision=lax.Precision.HIGHEST
    ).reshape(blocks, SPAN, heads_dev, HEADDIM)
    y_state = (jnp.exp(cum_acc)[..., None] * y_state).reshape(blocks, SPAN, slab)
    result = y_acc + y_state
    return result.astype(jnp.bfloat16).reshape(blocks * SPAN, slab)


def solution(mesh):
    placed = (P(("ctx", "head"), None), P(("ctx", "head"), None), P(), P(), P(), P(), P())
    return jax.shard_map(
        on_device, mesh=mesh, in_specs=placed, out_specs=P("ctx", "head"), check_vma=False
    )
```

```python
import jax
import jax.numpy as jnp
from jax import lax
from jax.sharding import PartitionSpec as P

HEADS = 256
HEADDIM = 64
STATE = 256
GROUPS = 8
CONV = 4
SPAN = 512


def on_device(conv_input, dt_raw, conv_weight, conv_bias, a_log, dt_bias, d_skip):
    f32 = jnp.float32
    head_count = lax.axis_size("head")
    ctx_count = lax.axis_size("ctx")
    heads_dev = HEADS // head_count
    repeat_count = head_count // GROUPS
    head_pos = lax.axis_index("head")
    rows = conv_input.shape[0]
    x_width = HEADS * HEADDIM
    slab = heads_dev * HEADDIM
    devices = ctx_count * head_count
    rim = lax.ppermute(
        conv_input[rows - (CONV - 1) :], ("ctx", "head"), [(i, i + 1) for i in range(devices - 1)]
    )
    padded = jnp.concatenate([rim, conv_input], 0)
    taps = conv_weight.astype(f32)

    def payload(target):
        group = target // repeat_count

        def pick(table):
            last = table.ndim - 1
            return jnp.concatenate(
                [
                    lax.dynamic_slice_in_dim(table, target * slab, slab, last),
                    lax.dynamic_slice_in_dim(table, x_width + group * STATE, STATE, last),
                    lax.dynamic_slice_in_dim(
                        table, x_width + (GROUPS + group) * STATE, STATE, last
                    ),
                ],
                last,
            )

        window, kernel = pick(padded), pick(taps)
        total = window[0:rows].astype(f32) * kernel[0]
        for k in range(1, CONV):
            total = total + window[k : k + rows].astype(f32) * kernel[k]
        act = jax.nn.silu(total + pick(conv_bias)).astype(jnp.bfloat16)
        steps = lax.dynamic_slice_in_dim(dt_raw, target * heads_dev, heads_dev, 1)
        return jnp.concatenate([act, steps], 1)

    rate = -jnp.exp(lax.dynamic_slice_in_dim(a_log, head_pos * heads_dev, heads_dev, 0))
    bias = lax.dynamic_slice_in_dim(dt_bias, head_pos * heads_dev, heads_dev, 0)
    skip = jnp.repeat(lax.dynamic_slice_in_dim(d_skip, head_pos * heads_dev, heads_dev, 0), HEADDIM)
    tri = lax.broadcasted_iota(jnp.int32, (SPAN, SPAN), 0) >= lax.broadcasted_iota(
        jnp.int32, (SPAN, SPAN), 1
    )
    pairs = head_count // 2
    blocks = pairs
    parity = head_pos % 2
    y_acc = jnp.zeros((blocks, SPAN, slab), f32)
    c_acc = jnp.zeros((blocks, SPAN, STATE), jnp.bfloat16)
    cum_acc = jnp.zeros((blocks, SPAN, heads_dev), f32)
    contrib_acc = jnp.zeros((blocks, STATE, slab), f32)
    done = []
    for m in range(blocks):
        same = [(i, 2 * ((i // 2 + m) % pairs) + i % 2) for i in range(head_count)]
        other = [(i, 2 * ((i // 2 + m) % pairs) + 1 - i % 2) for i in range(head_count)]
        t_same = 2 * ((head_pos // 2 + m) % pairs) + parity
        t_other = 2 * ((head_pos // 2 + m) % pairs) + 1 - parity
        p_same, p_other = payload(t_same), payload(t_other)
        if m >= 4:
            p_same, p_other, _ = lax.optimization_barrier((p_same, p_other, done[m - 4]))
        r_same = lax.ppermute(p_same, "head", same)
        r_other = lax.ppermute(p_other, "head", other)
        first = jnp.where(parity == 0, r_same, r_other)
        second = jnp.where(parity == 0, r_other, r_same)
        blk = jnp.concatenate([first, second], 0)
        k = (head_pos // 2 - m) % pairs
        x_now = blk[:, :slab]
        b_now = blk[:, slab : slab + STATE]
        c_now = blk[:, slab + STATE : slab + 2 * STATE]
        step_now = jax.nn.softplus(blk[:, slab + 2 * STATE :].astype(f32) + bias)
        cum_now = jnp.cumsum(rate * step_now, axis=0)
        gram = jnp.dot(c_now, b_now.T, preferred_element_type=f32)
        cum_t = cum_now.T
        decay = jnp.exp(jnp.where(tri[None], cum_t[:, :, None] - cum_t[:, None, :], -jnp.inf))
        mix = (gram[None] * decay * step_now.T[:, None, :]).astype(jnp.bfloat16)
        x_heads = x_now.reshape(SPAN, heads_dev, HEADDIM)
        y_block = jnp.einsum("hts,shp->thp", mix, x_heads, preferred_element_type=f32).reshape(
            SPAN, slab
        )
        y_now = y_block + skip * x_now.astype(f32)
        weight = jnp.exp(cum_now[-1][None, :] - cum_now) * step_now
        xw = (x_heads.astype(f32) * weight[:, :, None]).astype(jnp.bfloat16).reshape(SPAN, slab)
        contrib = jnp.einsum("sn,sc->nc", b_now, xw, preferred_element_type=f32)
        y_acc = lax.dynamic_update_index_in_dim(y_acc, y_now, k, 0)
        c_acc = lax.dynamic_update_index_in_dim(c_acc, c_now, k, 0)
        cum_acc = lax.dynamic_update_index_in_dim(cum_acc, cum_now, k, 0)
        contrib_acc = lax.dynamic_update_index_in_dim(contrib_acc, contrib, k, 0)
        done.append((contrib, y_now))

    block_totals = cum_acc[:, -1, :]
    state = jnp.zeros((STATE, slab), f32)
    entering = []
    for k in range(blocks):
        entering.append(state)
        fade = jnp.exp(jnp.repeat(block_totals[k], HEADDIM))
        state = state * fade[None, :] + contrib_acc[k]
    final = state
    entering = jnp.stack(entering)
    totals = jnp.sum(block_totals, axis=0)
    tail = jnp.broadcast_to(jnp.repeat(totals, HEADDIM)[None, :], (8, slab))
    gathered = lax.all_gather(jnp.concatenate([final, tail], 0), "ctx")
    shards = gathered.shape[0]
    position = lax.axis_index("ctx")
    finals = gathered[:, :STATE]
    shard_totals = gathered[:, STATE]
    before_shard = jnp.cumsum(shard_totals, axis=0) - shard_totals
    reach = jnp.sum(jnp.where(jnp.arange(shards)[:, None] < position, shard_totals, 0.0), axis=0)
    after_own = before_shard + shard_totals
    live = jnp.arange(shards)[:, None] < position
    weights = jnp.where(live, jnp.exp(jnp.where(live, reach[None] - after_own, 0.0)), 0.0)
    incoming = jnp.sum(weights[:, None, :] * finals, axis=0)
    before = jnp.concatenate(
        [jnp.zeros((1, heads_dev), f32), jnp.cumsum(block_totals, axis=0)[:-1]], 0
    )
    carried = jnp.exp(jnp.repeat(before, HEADDIM, axis=1))[:, None, :] * incoming[None]
    full_state = entering + carried
    grown = jnp.exp(jnp.repeat(cum_acc, HEADDIM, axis=2))
    y_state = grown * jnp.einsum(
        "bqn,bnc->bqc", c_acc.astype(f32), full_state, precision=lax.Precision.HIGHEST
    )
    result = y_acc + y_state
    return result.astype(jnp.bfloat16).reshape(blocks * SPAN, slab)


def solution(mesh):
    placed = (P(("ctx", "head"), None), P(("ctx", "head"), None), P(), P(), P(), P(), P())
    return jax.shard_map(
        on_device, mesh=mesh, in_specs=placed, out_specs=P("ctx", "head"), check_vma=False
    )
```

```python
import jax
import jax.numpy as jnp
from jax import lax
from jax.sharding import PartitionSpec as P

HEADS = 256
HEADDIM = 64
STATE = 256
GROUPS = 8
CONV = 4
SPAN = 512


def on_device(conv_input, dt_raw, conv_weight, conv_bias, a_log, dt_bias, d_skip):
    f32 = jnp.float32
    head_count = lax.axis_size("head")
    ctx_count = lax.axis_size("ctx")
    heads_dev = HEADS // head_count
    repeat_count = head_count // GROUPS
    head_pos = lax.axis_index("head")
    rows = conv_input.shape[0]
    x_width = HEADS * HEADDIM
    slab = heads_dev * HEADDIM
    devices = ctx_count * head_count
    rim = lax.ppermute(
        conv_input[rows - (CONV - 1) :], ("ctx", "head"), [(i, i + 1) for i in range(devices - 1)]
    )
    padded = jnp.concatenate([rim, conv_input], 0)
    taps = conv_weight.astype(f32)

    def payload(target):
        group = target // repeat_count

        def pick(table):
            last = table.ndim - 1
            return jnp.concatenate(
                [
                    lax.dynamic_slice_in_dim(table, target * slab, slab, last),
                    lax.dynamic_slice_in_dim(table, x_width + group * STATE, STATE, last),
                    lax.dynamic_slice_in_dim(
                        table, x_width + (GROUPS + group) * STATE, STATE, last
                    ),
                ],
                last,
            )

        window, kernel = pick(padded), pick(taps)
        total = window[0:rows].astype(f32) * kernel[0]
        for k in range(1, CONV):
            total = total + window[k : k + rows].astype(f32) * kernel[k]
        act = jax.nn.silu(total + pick(conv_bias)).astype(jnp.bfloat16)
        steps = lax.dynamic_slice_in_dim(dt_raw, target * heads_dev, heads_dev, 1)
        return jnp.concatenate([act, steps], 1)

    rate = -jnp.exp(lax.dynamic_slice_in_dim(a_log, head_pos * heads_dev, heads_dev, 0))
    bias = lax.dynamic_slice_in_dim(dt_bias, head_pos * heads_dev, heads_dev, 0)
    skip = jnp.repeat(lax.dynamic_slice_in_dim(d_skip, head_pos * heads_dev, heads_dev, 0), HEADDIM)
    tri = lax.broadcasted_iota(jnp.int32, (SPAN, SPAN), 0) >= lax.broadcasted_iota(
        jnp.int32, (SPAN, SPAN), 1
    )
    pairs = head_count // 2
    blocks = pairs
    parity = head_pos % 2
    y_acc = jnp.zeros((blocks, SPAN, slab), f32)
    c_acc = jnp.zeros((blocks, SPAN, STATE), jnp.bfloat16)
    cum_acc = jnp.zeros((blocks, SPAN, heads_dev), f32)
    contrib_acc = jnp.zeros((blocks, STATE, slab), f32)
    done = []
    for m in range(blocks):
        same = [(i, 2 * ((i // 2 + m) % pairs) + i % 2) for i in range(head_count)]
        other = [(i, 2 * ((i // 2 + m) % pairs) + 1 - i % 2) for i in range(head_count)]
        t_same = 2 * ((head_pos // 2 + m) % pairs) + parity
        t_other = 2 * ((head_pos // 2 + m) % pairs) + 1 - parity
        p_same, p_other = payload(t_same), payload(t_other)
        if m >= 5:
            p_same, p_other, _ = lax.optimization_barrier((p_same, p_other, done[m - 5]))
        r_same = lax.ppermute(p_same, "head", same)
        r_other = lax.ppermute(p_other, "head", other)
        first = jnp.where(parity == 0, r_same, r_other)
        second = jnp.where(parity == 0, r_other, r_same)
        blk = jnp.concatenate([first, second], 0)
        k = (head_pos // 2 - m) % pairs
        x_now = blk[:, :slab]
        b_now = blk[:, slab : slab + STATE]
        c_now = blk[:, slab + STATE : slab + 2 * STATE]
        step_now = jax.nn.softplus(blk[:, slab + 2 * STATE :].astype(f32) + bias)
        cum_now = jnp.cumsum(rate * step_now, axis=0)
        gram = jnp.dot(c_now, b_now.T, preferred_element_type=f32)
        cum_t = cum_now.T
        decay = jnp.exp(jnp.where(tri[None], cum_t[:, :, None] - cum_t[:, None, :], -jnp.inf))
        mix = (gram[None] * decay * step_now.T[:, None, :]).astype(jnp.bfloat16)
        x_heads = x_now.reshape(SPAN, heads_dev, HEADDIM)
        y_block = jnp.einsum("hts,shp->thp", mix, x_heads, preferred_element_type=f32).reshape(
            SPAN, slab
        )
        y_now = y_block + skip * x_now.astype(f32)
        weight = jnp.exp(cum_now[-1][None, :] - cum_now) * step_now
        xw = (x_heads.astype(f32) * weight[:, :, None]).astype(jnp.bfloat16).reshape(SPAN, slab)
        contrib = jnp.einsum("sn,sc->nc", b_now, xw, preferred_element_type=f32)
        y_acc = lax.dynamic_update_index_in_dim(y_acc, y_now, k, 0)
        c_acc = lax.dynamic_update_index_in_dim(c_acc, c_now, k, 0)
        cum_acc = lax.dynamic_update_index_in_dim(cum_acc, cum_now, k, 0)
        contrib_acc = lax.dynamic_update_index_in_dim(contrib_acc, contrib, k, 0)
        done.append((contrib, y_now))

    block_totals = cum_acc[:, -1, :]
    state = jnp.zeros((STATE, slab), f32)
    entering = []
    for k in range(blocks):
        entering.append(state)
        fade = jnp.exp(jnp.repeat(block_totals[k], HEADDIM))
        state = state * fade[None, :] + contrib_acc[k]
    final = state
    entering = jnp.stack(entering)
    totals = jnp.sum(block_totals, axis=0)
    tail = jnp.broadcast_to(jnp.repeat(totals, HEADDIM)[None, :], (8, slab))
    gathered = lax.all_gather(jnp.concatenate([final, tail], 0), "ctx")
    shards = gathered.shape[0]
    position = lax.axis_index("ctx")
    finals = gathered[:, :STATE]
    shard_totals = gathered[:, STATE]
    before_shard = jnp.cumsum(shard_totals, axis=0) - shard_totals
    reach = jnp.sum(jnp.where(jnp.arange(shards)[:, None] < position, shard_totals, 0.0), axis=0)
    after_own = before_shard + shard_totals
    live = jnp.arange(shards)[:, None] < position
    weights = jnp.where(live, jnp.exp(jnp.where(live, reach[None] - after_own, 0.0)), 0.0)
    incoming = jnp.sum(weights[:, None, :] * finals, axis=0)
    before = jnp.concatenate(
        [jnp.zeros((1, heads_dev), f32), jnp.cumsum(block_totals, axis=0)[:-1]], 0
    )
    carried = jnp.exp(jnp.repeat(before, HEADDIM, axis=1))[:, None, :] * incoming[None]
    full_state = entering + carried
    grown = jnp.exp(jnp.repeat(cum_acc, HEADDIM, axis=2))
    y_state = grown * jnp.einsum(
        "bqn,bnc->bqc", c_acc.astype(f32), full_state, precision=lax.Precision.HIGHEST
    )
    result = y_acc + y_state
    return result.astype(jnp.bfloat16).reshape(blocks * SPAN, slab)


def solution(mesh):
    placed = (P(("ctx", "head"), None), P(("ctx", "head"), None), P(), P(), P(), P(), P())
    return jax.shard_map(
        on_device, mesh=mesh, in_specs=placed, out_specs=P("ctx", "head"), check_vma=False
    )
```
